128 devices in a mesh: tm: 64 (over z, y, x), tile: 2 (over core).
Axes of the slice: x: 4, y: 4, z: 4, core: 2. Of those that a mesh axis runs over, the one named last changes fastest.
Arguments:
- pivot_inverse: bfloat16 [64, 1024, 1024], P('tm', 'tile'), may hold values from -0.2 to 8.2, as said below
- mult_left: bfloat16 [64, 1024, 1024], P('tm', 'tile'), may hold values from -0.09375 to 0.09375
- mult_right: bfloat16 [64, 1024, 1024], P('tm', 'tile'), may hold values from -0.09375 to 0.09375
- mult_tip: bfloat16 [64, 64, 1024], P('tm', 'tile'), may hold values from -0.09375 to 0.09375
- root_cross: bfloat16 [64, 1024], P(None, 'tile'), may hold values from -0.59765625 to 0.59765625
- root_tip: bfloat16 [64, 64], replicated, may hold values from -0.2 to 8.2, as said below
Outputs:
- marginal_cov: bfloat16 [64, 1024, 1024], P('tm', 'tile')
- cross_cov: bfloat16 [64, 1024, 2048], P('tm', 'tile')
- tip_cov: bfloat16 [64, 64, 1024], P('tm', None, 'tile')
The draws below stay inside these ranges and needn't reach their ends.
Inputs may be any that keep to these rules, and one draw needn't show every extreme that they name: `pivot_inverse`: each of the 64 matrices is symmetric. `root_tip`: symmetric.
All inputs are finite; a program needn't handle non-finite values.
Results may differ from the reference program's by a relative error of at most 0.006.
Values may be sent and summed in bfloat16 or wider, within the bound.
No kernel may reach another device: no remote copies, remote signals or barrier semaphores. Data moves between devices by JAX's collectives and lax.ppermute only.
A program may use at most 128 MiB of HBM per device.

```python
import jax
import jax.numpy as jnp
from jax import lax

B = 1024
A = 64
STEPS = 64
LEVELS = 6


def symmetric_draw(key, count, order):
    key_rough, key_main = jax.random.split(key, 2)
    rough = jnp.clip(jax.random.normal(key_rough, (count, order, order), jnp.float32), -4.0, 4.0) * 0.01
    paired = (rough + jnp.swapaxes(rough, 1, 2)) * 0.5
    main = jax.random.uniform(key_main, (count, order), jnp.float32, 0.75, 2.0)
    rows = lax.broadcasted_iota(jnp.int32, (order, order), 0)
    cols = lax.broadcasted_iota(jnp.int32, (order, order), 1)
    unit = (rows == cols).astype(jnp.float32)
    matrix = paired * (1.0 - unit) + unit * main[:, :, None]
    return matrix


def draw_pivot_inverse(key, part):
    return symmetric_draw(jax.random.fold_in(key, 11), STEPS, B).astype(jnp.bfloat16)


def draw_root_tip(key, part):
    return symmetric_draw(jax.random.fold_in(key, 23), 1, A)[0].astype(jnp.bfloat16)


def block_scale(own_key, shape, cuts, low, largest):
    def one(position, parts):
        steps = jax.random.uniform(jax.random.fold_in(jax.random.fold_in(own_key, 6), position), (parts,), jnp.float32, low / len(cuts), largest / len(cuts))
        return jnp.repeat(jnp.exp(steps), shape[position] // parts).reshape((-1,) + (1,) * (len(shape) - position - 1))

    loudness = one(*cuts[0])
    for cut in cuts[1:]:
        loudness = loudness * one(*cut)
    return loudness


def normal_values(rng, extent, width, bound, cuts=(), held_as=jnp.bfloat16):
    array = jax.random.normal(rng, extent, jnp.float32) * width
    if len(cuts) > 0:
        array = block_scale(rng, extent, cuts, -0.22, 0.18) * array
    return jnp.clip(array, min=-bound, max=bound).astype(held_as)


def setup_inputs(seed: int = 0) -> dict:
    key_list = jax.random.split(jax.random.key(seed), 7)
    pivot_inverse = draw_pivot_inverse(jax.random.fold_in(key_list[6], 71), 0)
    mult_left = normal_values(key_list[1], (STEPS, B, B), (4 * B + 2 * A) ** -0.5, 0.09375, ((0, 64), (1, 2)))
    mult_right = normal_values(key_list[2], (STEPS, B, B), (4 * B + 2 * A) ** -0.5, 0.09375, ((0, 64), (1, 2)))
    mult_tip = normal_values(key_list[3], (STEPS, A, B), (4 * B + 2 * A) ** -0.5, 0.09375, ((0, 64), (1, 2)))
    root_cross = normal_values(key_list[4], (A, B), 0.1, 0.59765625, ((1, 2),))
    root_tip = draw_root_tip(jax.random.fold_in(key_list[6], 71), 0)
    return dict(pivot_inverse=pivot_inverse, mult_left=mult_left, mult_right=mult_right, mult_tip=mult_tip, root_cross=root_cross, root_tip=root_tip)


def product(left_matrix, right_matrix):
    return jnp.dot(left_matrix, right_matrix, preferred_element_type=jnp.float32)


def pivots_at(level_index):
    return [block for block in range(STEPS) if block % 2 ** (level_index + 1) == 2 ** level_index - 1]


def reference(pivot_inverse, mult_left, mult_right, mult_tip, root_cross, root_tip):
    offset = 5 % STEPS
    pivot_inverse = jnp.roll(pivot_inverse, offset, axis=0)
    mult_left = jnp.roll(mult_left, offset, axis=0)
    mult_right = jnp.roll(mult_right, offset, axis=0)
    mult_tip = jnp.roll(mult_tip, offset, axis=0)
    last = STEPS - 1
    nodes = pivot_inverse.shape[1]
    zero_block = jnp.zeros((nodes, nodes), jnp.bfloat16)
    zero_tip = jnp.zeros((A, nodes), jnp.bfloat16)
    diagonal = {last: pivot_inverse[last]}
    tip_cross = {last: root_cross}
    self_left = {last: zero_block}
    self_right = {last: zero_block}
    near_left = {last: zero_block}
    near_right = {last: zero_block}
    for level_index in reversed(range(LEVELS)):
        distance = 2 ** level_index
        for block in pivots_at(level_index):
            right_id = block + distance
            left_id = block - distance
            if block >= distance:
                left_diag = diagonal[left_id]
                left_tip = tip_cross[left_id]
                if left_id % 2 ** (level_index + 2) == 2 ** (level_index + 1) - 1:
                    left_right = self_right[left_id]
                    right_left = near_right[left_id]
                else:
                    left_right = near_left[right_id]
                    right_left = self_left[right_id]
            else:
                left_diag = zero_block
                left_tip = zero_tip
                left_right = zero_block
                right_left = zero_block
            g_left = mult_left[block]
            g_right = mult_right[block]
            g_tip = mult_tip[block]
            near_a = product(left_diag, g_left) + product(left_right, g_right) + product(left_tip.T, g_tip)
            near_b = product(right_left, g_left) + product(diagonal[right_id], g_right) + product(tip_cross[right_id].T, g_tip)
            tip_part = product(left_tip, g_left) + product(tip_cross[right_id], g_right) + product(root_tip, g_tip)
            fresh_a = (-near_a).astype(jnp.bfloat16)
            fresh_b = (-near_b).astype(jnp.bfloat16)
            fresh_tip = (-tip_part).astype(jnp.bfloat16)
            own_a = fresh_a.T
            own_b = fresh_b.T
            total = product(own_a, g_left) + product(own_b, g_right) + product(fresh_tip.T, g_tip)
            diagonal[block] = (pivot_inverse[block].astype(jnp.float32) - total).astype(jnp.bfloat16)
            tip_cross[block] = fresh_tip
            near_left[block] = fresh_a
            near_right[block] = fresh_b
            self_left[block] = own_a
            self_right[block] = own_b
    marginal = jnp.stack([diagonal[block_id] for block_id in range(STEPS)])
    crossing = jnp.stack([jnp.concatenate([self_left[block_id], self_right[block_id]], axis=1) for block_id in range(STEPS)])
    tip_blocks = jnp.stack([tip_cross[block_id] for block_id in range(STEPS)])
    marginal = jnp.roll(marginal, -offset, axis=0)
    crossing = jnp.roll(crossing, -offset, axis=0)
    tip_blocks = jnp.roll(tip_blocks, -offset, axis=0)
    return (marginal, crossing, tip_blocks)
```

```python
import numpy as np

import jax
import jax.numpy as jnp
from jax import lax
from jax.sharding import PartitionSpec as P


def product(left_matrix, right_matrix):
    return jnp.dot(left_matrix, right_matrix, preferred_element_type=jnp.float32)


def level_of(block, steps, levels):
    if block == steps - 1:
        return levels
    level = 0
    while (block >> level) & 1:
        level += 1
    return level


def plan(steps, levels, offset):
    where_is = lambda block: (block - offset) % steps
    levels_plan = {}
    for level_index in reversed(range(levels)):
        distance = 2**level_index
        crit_from_left, crit_from_right = [], []
        pre_from_left, pre_from_right = [], []
        c_left = [False] * steps
        active = [False] * steps
        for block in range(steps):
            if block % (2 * distance) != distance - 1:
                continue
            active[where_is(block)] = True
            left_id, right_id = block - distance, block + distance
            if left_id >= 0 and level_of(left_id, steps, levels) == level_index + 1:
                c_left[where_is(block)] = True
                crit_from_left.append((where_is(left_id), where_is(block)))
                pre_from_right.append((where_is(right_id), where_is(block)))
            else:
                crit_from_right.append((where_is(right_id), where_is(block)))
                if left_id >= 0:
                    pre_from_left.append((where_is(left_id), where_is(block)))
        levels_plan[level_index] = dict(
            crit_from_left=crit_from_left,
            crit_from_right=crit_from_right,
            pre_from_left=pre_from_left,
            pre_from_right=pre_from_right,
            c_left=c_left,
            active=active,
        )
    return levels_plan


def pick(flag, if_true, if_false):
    if if_true is None:
        return if_false
    if if_false is None:
        return if_true
    return jnp.where(flag, if_true, if_false)


def send(values, pairs):
    if not pairs:
        return None
    return lax.ppermute(values, "tm", pairs)


def tile_transpose(rows):
    turned = lax.all_to_all(rows[None], "tile", split_axis=2, concat_axis=1, tiled=True)
    return turned[0].T


def body(pivot_inverse, mult_left, mult_right, mult_tip, root_cross, root_tip):
    steps = lax.axis_size("tm")
    levels = steps.bit_length() - 1
    offset = 5 % steps
    levels_plan = plan(steps, levels, offset)
    position = lax.axis_index("tm")
    tile_index = lax.axis_index("tile")
    tile_rows = pivot_inverse.shape[1]

    own_left = mult_left[0]
    own_right = mult_right[0]
    inverse_rows = pivot_inverse[0]
    full_left = lax.all_gather(own_left, "tile", axis=0, tiled=True)
    full_right = lax.all_gather(own_right, "tile", axis=0, tiled=True)
    full_tip = lax.all_gather(mult_tip[0], "tile", axis=0, tiled=True)
    tip_cols = lax.dynamic_slice_in_dim(full_tip, tile_index * tile_rows, tile_rows, 1)
    tip_own = product(root_tip, tip_cols)

    zero_rows = jnp.zeros_like(inverse_rows)
    zero_tip = jnp.zeros_like(root_cross)

    def table(values):
        return jnp.asarray(np.array(values, dtype=bool))[position]

    up_diag, up_tip, up_self_left, up_self_right = inverse_rows, root_cross, zero_rows, zero_rows
    state_diag, state_tip = inverse_rows, root_cross
    state_cross = jnp.zeros((tile_rows, 2 * inverse_rows.shape[1]), inverse_rows.dtype)
    history = {levels: (state_diag, state_tip)}

    for level_index in reversed(range(levels)):
        step_plan = levels_plan[level_index]
        c_left = table(step_plan["c_left"])
        active = table(step_plan["active"])

        from_left = send((up_diag, up_tip, up_self_right), step_plan["crit_from_left"])
        from_right = send((up_diag, up_tip, up_self_left), step_plan["crit_from_right"])
        near_diag = pick(c_left, *(None if r is None else r[0] for r in (from_left, from_right)))
        near_tip = pick(c_left, *(None if r is None else r[1] for r in (from_left, from_right)))
        cross = pick(c_left, *(None if r is None else r[2] for r in (from_left, from_right)))

        older = history.get(level_index + 2)
        if older is None:
            far_diag, far_tip = zero_rows, zero_tip
        else:
            g_left = send(older, step_plan["pre_from_left"])
            g_right = send(older, step_plan["pre_from_right"])
            if g_left is None and g_right is None:
                far_diag, far_tip = zero_rows, zero_tip
            else:
                far_diag = pick(c_left, *(None if r is None else r[0] for r in (g_right, g_left)))
                far_tip = pick(c_left, *(None if r is None else r[1] for r in (g_right, g_left)))

        first = jnp.where(c_left, full_left, full_right)
        second = jnp.where(c_left, full_right, full_left)
        first_rows = jnp.where(c_left, own_left, own_right)
        second_rows = jnp.where(c_left, own_right, own_left)
        stacked = jnp.concatenate([first, second, full_tip], axis=0)

        cross_turned = tile_transpose(cross)
        operand = jnp.concatenate(
            [
                jnp.concatenate([near_diag, cross, near_tip.T], axis=1),
                jnp.concatenate([cross_turned, far_diag, far_tip.T], axis=1),
            ],
            axis=0,
        )
        fresh_both = (-product(operand, stacked)).astype(jnp.bfloat16)
        fresh_near = fresh_both[:tile_rows]
        fresh_far = fresh_both[tile_rows:]
        tip_part = product(near_tip, first_rows) + product(far_tip, second_rows)
        tip_sum = lax.psum_scatter(tip_part, "tile", scatter_dimension=1, tiled=True)
        fresh_tip = (-(tip_sum + tip_own)).astype(jnp.bfloat16)
        turned = lax.all_to_all(
            jnp.stack([fresh_near, fresh_far]), "tile", split_axis=2, concat_axis=1, tiled=True
        )
        own_near = turned[0].T
        own_far = turned[1].T
        total = product(jnp.concatenate([own_near, own_far, fresh_tip.T], axis=1), stacked)
        fresh_diag = (inverse_rows.astype(jnp.float32) - total).astype(jnp.bfloat16)
        self_left = jnp.where(c_left, own_near, own_far)
        self_right = jnp.where(c_left, own_far, own_near)

        state_diag = jnp.where(active, fresh_diag, state_diag)
        state_tip = jnp.where(active, fresh_tip, state_tip)
        state_cross = jnp.where(active, jnp.concatenate([self_left, self_right], axis=1), state_cross)
        history[level_index] = (state_diag, state_tip)
        up_diag, up_tip, up_self_left, up_self_right = fresh_diag, fresh_tip, self_left, self_right

    return (state_diag[None], state_cross[None], state_tip[None])


def solution(mesh):
    placed = (
        P("tm", "tile", None),
        P("tm", "tile", None),
        P("tm", "tile", None),
        P("tm", "tile", None),
        P(None, "tile"),
        P(),
    )
    return jax.shard_map(
        body,
        mesh=mesh,
        in_specs=placed,
        out_specs=(P("tm", "tile", None), P("tm", "tile", None), P("tm", None, "tile")),
        check_vma=False,
    )
```

```python
import numpy as np

import jax
import jax.numpy as jnp
from jax import lax
from jax.sharding import PartitionSpec as P


def product(left_matrix, right_matrix):
    return jnp.dot(left_matrix, right_matrix, preferred_element_type=jnp.float32)


def level_of(block, steps, levels):
    if block == steps - 1:
        return levels
    level = 0
    while (block >> level) & 1:
        level += 1
    return level


def plan(steps, levels, offset):
    where_is = lambda block: (block - offset) % steps
    levels_plan = {}
    for level_index in reversed(range(levels)):
        distance = 2**level_index
        crit_from_left, crit_from_right = [], []
        pre_from_left, pre_from_right = [], []
        c_left = [False] * steps
        active = [False] * steps
        for block in range(steps):
            if block % (2 * distance) != distance - 1:
                continue
            active[where_is(block)] = True
            left_id, right_id = block - distance, block + distance
            if left_id >= 0 and level_of(left_id, steps, levels) == level_index + 1:
                c_left[where_is(block)] = True
                crit_from_left.append((where_is(left_id), where_is(block)))
                pre_from_right.append((where_is(right_id), where_is(block)))
            else:
                crit_from_right.append((where_is(right_id), where_is(block)))
                if left_id >= 0:
                    pre_from_left.append((where_is(left_id), where_is(block)))
        levels_plan[level_index] = dict(
            crit_from_left=crit_from_left,
            crit_from_right=crit_from_right,
            pre_from_left=pre_from_left,
            pre_from_right=pre_from_right,
            c_left=c_left,
            active=active,
        )
    return levels_plan


def pick(flag, if_true, if_false):
    if if_true is None:
        return if_false
    if if_false is None:
        return if_true
    return jnp.where(flag, if_true, if_false)


def send(values, pairs):
    if not pairs:
        return None
    return lax.ppermute(values, "tm", pairs)


def swap_tiles(values):
    return lax.ppermute(values, "tile", [(0, 1), (1, 0)])


def tile_transpose(blocks, is_first):
    half = blocks.shape[1]
    left, right = blocks[:, :, :half], blocks[:, :, half:]
    mine = jnp.where(is_first, left, right)
    got = swap_tiles(jnp.where(is_first, right, left))
    top = jnp.where(is_first, mine, got)
    bottom = jnp.where(is_first, got, mine)
    return jnp.concatenate([jnp.swapaxes(top, 1, 2), jnp.swapaxes(bottom, 1, 2)], axis=2)


def join_tiles(halves, is_first):
    got = swap_tiles(halves)
    return jnp.where(is_first, jnp.concatenate([halves, got], axis=-1), jnp.concatenate([got, halves], axis=-1))


def body(pivot_inverse, mult_left, mult_right, mult_tip, root_cross, root_tip):
    steps = lax.axis_size("tm")
    levels = steps.bit_length() - 1
    offset = 5 % steps
    levels_plan = plan(steps, levels, offset)
    position = lax.axis_index("tm")
    tile_index = lax.axis_index("tile")
    is_first = tile_index == 0
    tile_rows = pivot_inverse.shape[1]

    def table(values):
        return jnp.asarray(np.array(values, dtype=bool))[position]

    own_role = [False] * steps
    for level_index, step_plan in levels_plan.items():
        for where_at in range(steps):
            if step_plan["active"][where_at]:
                own_role[where_at] = step_plan["c_left"][where_at]
    role = table(own_role)

    own_left = mult_left[0]
    own_right = mult_right[0]
    inverse_rows = pivot_inverse[0]
    full_left = lax.all_gather(own_left, "tile", axis=0, tiled=True)
    full_right = lax.all_gather(own_right, "tile", axis=0, tiled=True)
    full_tip = lax.all_gather(mult_tip[0], "tile", axis=0, tiled=True)
    first = jnp.where(role, full_left, full_right)
    second = jnp.where(role, full_right, full_left)
    stacked = jnp.concatenate([first, second, full_tip], axis=0)
    col_start = tile_index * tile_rows
    first_cols = lax.dynamic_slice_in_dim(first, col_start, tile_rows, 1)
    second_cols = lax.dynamic_slice_in_dim(second, col_start, tile_rows, 1)
    tip_cols = lax.dynamic_slice_in_dim(full_tip, col_start, tile_rows, 1)
    tip_own = product(root_tip, tip_cols)

    zero_rows = jnp.zeros_like(inverse_rows)
    zero_tip = jnp.zeros_like(root_cross)

    up_diag, up_tip, up_self_left, up_self_right = inverse_rows, root_cross, zero_rows, zero_rows
    state_diag, state_tip = inverse_rows, root_cross
    state_cross = jnp.zeros((tile_rows, 2 * inverse_rows.shape[1]), inverse_rows.dtype)
    history = {levels: (state_diag, state_tip)}

    for level_index in reversed(range(levels)):
        step_plan = levels_plan[level_index]
        active = table(step_plan["active"])

        from_left = send((up_diag, up_tip, up_self_right), step_plan["crit_from_left"])
        from_right = send((up_diag, up_tip, up_self_left), step_plan["crit_from_right"])
        near_diag = pick(role, *(None if r is None else r[0] for r in (from_left, from_right)))
        near_tip = pick(role, *(None if r is None else r[1] for r in (from_left, from_right)))
        cross = pick(role, *(None if r is None else r[2] for r in (from_left, from_right)))

        older = history.get(level_index + 2)
        far_diag, far_tip = zero_rows, zero_tip
        if older is not None:
            g_left = send(older, step_plan["pre_from_left"])
            g_right = send(older, step_plan["pre_from_right"])
            if g_left is not None or g_right is not None:
                far_diag = pick(role, *(None if r is None else r[0] for r in (g_right, g_left)))
                far_tip = pick(role, *(None if r is None else r[1] for r in (g_right, g_left)))

        cross_turned = tile_transpose(cross[None], is_first)[0]
        tips_full = join_tiles(jnp.stack([near_tip, far_tip]), is_first)
        operand = jnp.concatenate(
            [
                jnp.concatenate([near_diag, cross, near_tip.T], axis=1),
                jnp.concatenate([cross_turned, far_diag, far_tip.T], axis=1),
            ],
            axis=0,
        )
        fresh_both = (-product(operand, stacked)).astype(jnp.bfloat16)
        fresh_near = fresh_both[:tile_rows]
        fresh_far = fresh_both[tile_rows:]
        tip_y = product(tips_full[0], first_cols) + product(tips_full[1], second_cols) + tip_own
        fresh_tip = (-tip_y).astype(jnp.bfloat16)
        turned = tile_transpose(jnp.stack([fresh_near, fresh_far]), is_first)
        own_near = turned[0]
        own_far = turned[1]
        total = product(jnp.concatenate([own_near, own_far, fresh_tip.T], axis=1), stacked)
        fresh_diag = (inverse_rows.astype(jnp.float32) - total).astype(jnp.bfloat16)
        self_left = jnp.where(role, own_near, own_far)
        self_right = jnp.where(role, own_far, own_near)

        state_diag = jnp.where(active, fresh_diag, state_diag)
        state_tip = jnp.where(active, fresh_tip, state_tip)
        state_cross = jnp.where(active, jnp.concatenate([self_left, self_right], axis=1), state_cross)
        history[level_index] = (state_diag, state_tip)
        up_diag, up_tip, up_self_left, up_self_right = fresh_diag, fresh_tip, self_left, self_right

    return (state_diag[None], state_cross[None], state_tip[None])


def solution(mesh):
    placed = (
        P("tm", "tile", None),
        P("tm", "tile", None),
        P("tm", "tile", None),
        P("tm", "tile", None),
        P(None, "tile"),
        P(),
    )
    return jax.shard_map(
        body,
        mesh=mesh,
        in_specs=placed,
        out_specs=(P("tm", "tile", None), P("tm", "tile", None), P("tm", None, "tile")),
        check_vma=False,
    )
```

```python
import numpy as np

import jax
import jax.numpy as jnp
from jax import lax
from jax.sharding import PartitionSpec as P


def product(left_matrix, right_matrix):
    return jnp.dot(left_matrix, right_matrix, preferred_element_type=jnp.float32)


def level_of(block, steps, levels):
    if block == steps - 1:
        return levels
    level = 0
    while (block >> level) & 1:
        level += 1
    return level


def plan(steps, levels, offset):
    where_is = lambda block: (block - offset) % steps
    levels_plan = {}
    for level_index in reversed(range(levels)):
        distance = 2**level_index
        crit_from_left, crit_from_right = [], []
        pre_from_left, pre_from_right = [], []
        c_left = [False] * steps
        active = [False] * steps
        for block in range(steps):
            if block % (2 * distance) != distance - 1:
                continue
            active[where_is(block)] = True
            left_id, right_id = block - distance, block + distance
            if left_id >= 0 and level_of(left_id, steps, levels) == level_index + 1:
                c_left[where_is(block)] = True
                crit_from_left.append((where_is(left_id), where_is(block)))
                pre_from_right.append((where_is(right_id), where_is(block)))
            else:
                crit_from_right.append((where_is(right_id), where_is(block)))
                if left_id >= 0:
                    pre_from_left.append((where_is(left_id), where_is(block)))
        levels_plan[level_index] = dict(
            crit_from_left=crit_from_left,
            crit_from_right=crit_from_right,
            pre_from_left=pre_from_left,
            pre_from_right=pre_from_right,
            c_left=c_left,
            active=active,
        )
    return levels_plan


def pick(flag, if_true, if_false):
    if if_true is None:
        return if_false
    if if_false is None:
        return if_true
    return jnp.where(flag, if_true, if_false)


def send(values, pairs):
    if not pairs:
        return None
    return lax.ppermute(values, "tm", pairs)


def swap_tiles(values):
    return lax.ppermute(values, "tile", [(0, 1), (1, 0)])


def tile_transpose(blocks, is_first):
    half = blocks.shape[1]
    left, right = blocks[:, :, :half], blocks[:, :, half:]
    mine = jnp.where(is_first, left, right)
    got = swap_tiles(jnp.where(is_first, right, left))
    top = jnp.where(is_first, mine, got)
    bottom = jnp.where(is_first, got, mine)
    return jnp.concatenate([jnp.swapaxes(top, 1, 2), jnp.swapaxes(bottom, 1, 2)], axis=2)


def join_tiles(halves, is_first, axis=-1):
    got = swap_tiles(halves)
    return jnp.where(
        is_first, jnp.concatenate([halves, got], axis=axis), jnp.concatenate([got, halves], axis=axis)
    )


def body(pivot_inverse, mult_left, mult_right, mult_tip, root_cross, root_tip):
    steps = lax.axis_size("tm")
    levels = steps.bit_length() - 1
    offset = 5 % steps
    levels_plan = plan(steps, levels, offset)
    position = lax.axis_index("tm")
    tile_index = lax.axis_index("tile")
    is_first = tile_index == 0
    tile_rows = pivot_inverse.shape[1]

    def table(values):
        return jnp.asarray(np.array(values, dtype=bool))[position]

    own_role = [False] * steps
    for level_index, step_plan in levels_plan.items():
        for where_at in range(steps):
            if step_plan["active"][where_at]:
                own_role[where_at] = step_plan["c_left"][where_at]
    role = table(own_role)

    own_left = mult_left[0]
    own_right = mult_right[0]
    inverse_rows = pivot_inverse[0]
    full_left = join_tiles(own_left, is_first, axis=0)
    full_right = join_tiles(own_right, is_first, axis=0)
    full_tip = join_tiles(mult_tip[0], is_first, axis=0)
    first = jnp.where(role, full_left, full_right)
    second = jnp.where(role, full_right, full_left)
    stacked = jnp.concatenate([first, second, full_tip], axis=0)
    col_start = tile_index * tile_rows
    first_cols = lax.dynamic_slice_in_dim(first, col_start, tile_rows, 1)
    second_cols = lax.dynamic_slice_in_dim(second, col_start, tile_rows, 1)
    tip_cols = lax.dynamic_slice_in_dim(full_tip, col_start, tile_rows, 1)
    tip_own = product(root_tip, tip_cols)

    zero_rows = jnp.zeros_like(inverse_rows)
    zero_tip = jnp.zeros_like(root_cross)

    up_diag, up_tip, up_self_left, up_self_right = inverse_rows, root_cross, None, None
    state_diag, state_tip = inverse_rows, root_cross
    state_cross = jnp.zeros((tile_rows, 2 * inverse_rows.shape[1]), inverse_rows.dtype)
    history = {levels: (state_diag, state_tip)}

    for level_index in reversed(range(levels)):
        step_plan = levels_plan[level_index]
        active = table(step_plan["active"])

        from_left = send((up_diag, up_tip), step_plan["crit_from_left"])
        from_right = send((up_diag, up_tip), step_plan["crit_from_right"])
        near_diag = pick(role, *(None if r is None else r[0] for r in (from_left, from_right)))
        near_tip = pick(role, *(None if r is None else r[1] for r in (from_left, from_right)))
        if up_self_left is None:
            cross = None
        else:
            cross_left = send(up_self_right, step_plan["crit_from_left"])
            cross_right = send(up_self_left, step_plan["crit_from_right"])
            cross = pick(role, cross_left, cross_right)

        older = history.get(level_index + 2)
        far_diag, far_tip = zero_rows, zero_tip
        if older is not None:
            g_left = send(older, step_plan["pre_from_left"])
            g_right = send(older, step_plan["pre_from_right"])
            if g_left is not None or g_right is not None:
                far_diag = pick(role, *(None if r is None else r[0] for r in (g_right, g_left)))
                far_tip = pick(role, *(None if r is None else r[1] for r in (g_right, g_left)))

        tips_full = join_tiles(jnp.stack([near_tip, far_tip]), is_first)
        if cross is None:
            near_operand = jnp.concatenate([near_diag, near_tip.T], axis=1)
            near_mult = jnp.concatenate([first, full_tip], axis=0)
            far_operand = jnp.concatenate([far_diag, far_tip.T], axis=1)
            far_mult = jnp.concatenate([second, full_tip], axis=0)
        else:
            cross_turned = tile_transpose(cross[None], is_first)[0]
            near_operand = jnp.concatenate([near_diag, cross, near_tip.T], axis=1)
            near_mult = stacked
            far_operand = jnp.concatenate([cross_turned, far_diag, far_tip.T], axis=1)
            far_mult = stacked
        fresh_far = (-product(far_operand, far_mult)).astype(jnp.bfloat16)
        fresh_near = (-product(near_operand, near_mult)).astype(jnp.bfloat16)
        tip_y = product(tips_full[0], first_cols) + product(tips_full[1], second_cols) + tip_own
        fresh_tip = (-tip_y).astype(jnp.bfloat16)
        turned = tile_transpose(jnp.stack([fresh_near, fresh_far]), is_first)
        own_near = turned[0]
        own_far = turned[1]
        total = product(jnp.concatenate([own_near, own_far, fresh_tip.T], axis=1), stacked)
        fresh_diag = (inverse_rows.astype(jnp.float32) - total).astype(jnp.bfloat16)
        self_left = jnp.where(role, own_near, own_far)
        self_right = jnp.where(role, own_far, own_near)

        state_diag = jnp.where(active, fresh_diag, state_diag)
        state_tip = jnp.where(active, fresh_tip, state_tip)
        state_cross = jnp.where(active, jnp.concatenate([self_left, self_right], axis=1), state_cross)
        history[level_index] = (state_diag, state_tip)
        up_diag, up_tip, up_self_left, up_self_right = fresh_diag, fresh_tip, self_left, self_right

    return (state_diag[None], state_cross[None], state_tip[None])


def solution(mesh):
    placed = (
        P("tm", "tile", None),
        P("tm", "tile", None),
        P("tm", "tile", None),
        P("tm", "tile", None),
        P(None, "tile"),
        P(),
    )
    return jax.shard_map(
        body,
        mesh=mesh,
        in_specs=placed,
        out_specs=(P("tm", "tile", None), P("tm", "tile", None), P("tm", None, "tile")),
        check_vma=False,
    )
```

```python
import numpy as np

import jax
import jax.numpy as jnp
from jax import lax
from jax.sharding import PartitionSpec as P


def product(left_matrix, right_matrix):
    return jnp.dot(left_matrix, right_matrix, preferred_element_type=jnp.float32)


def level_of(block, steps, levels):
    if block == steps - 1:
        return levels
    level = 0
    while (block >> level) & 1:
        level += 1
    return level


def plan(steps, levels, offset):
    where_is = lambda block: (block - offset) % steps
    levels_plan = {}
    for level_index in reversed(range(levels)):
        distance = 2**level_index
        crit_from_left, crit_from_right = [], []
        pre_from_left, pre_from_right = [], []
        c_left = [False] * steps
        active = [False] * steps
        for block in range(steps):
            if block % (2 * distance) != distance - 1:
                continue
            active[where_is(block)] = True
            left_id, right_id = block - distance, block + distance
            if left_id >= 0 and level_of(left_id, steps, levels) == level_index + 1:
                c_left[where_is(block)] = True
                crit_from_left.append((where_is(left_id), where_is(block)))
                pre_from_right.append((where_is(right_id), where_is(block)))
            else:
                crit_from_right.append((where_is(right_id), where_is(block)))
                if left_id >= 0:
                    pre_from_left.append((where_is(left_id), where_is(block)))
        levels_plan[level_index] = dict(
            crit_from_left=crit_from_left,
            crit_from_right=crit_from_right,
            pre_from_left=pre_from_left,
            pre_from_right=pre_from_right,
            c_left=c_left,
            active=active,
        )
    return levels_plan


def pick(flag, if_true, if_false):
    if if_true is None:
        return if_false
    if if_false is None:
        return if_true
    return jnp.where(flag, if_true, if_false)


def send(values, pairs):
    if not pairs:
        return None
    return lax.ppermute(values, "tm", pairs)


def swap_tiles(values):
    return lax.ppermute(values, "tile", [(0, 1), (1, 0)])


def tile_transpose(blocks, is_first):
    half = blocks.shape[1]
    left, right = blocks[:, :, :half], blocks[:, :, half:]
    mine = jnp.where(is_first, left, right)
    got = swap_tiles(jnp.where(is_first, right, left))
    top = jnp.where(is_first, mine, got)
    bottom = jnp.where(is_first, got, mine)
    return jnp.concatenate([jnp.swapaxes(top, 1, 2), jnp.swapaxes(bottom, 1, 2)], axis=2)


def join_tiles(halves, is_first, axis=-1):
    got = swap_tiles(halves)
    return jnp.where(
        is_first, jnp.concatenate([halves, got], axis=axis), jnp.concatenate([got, halves], axis=axis)
    )


def body(pivot_inverse, mult_left, mult_right, mult_tip, root_cross, root_tip):
    steps = lax.axis_size("tm")
    levels = steps.bit_length() - 1
    offset = 5 % steps
    levels_plan = plan(steps, levels, offset)
    position = lax.axis_index("tm")
    tile_index = lax.axis_index("tile")
    is_first = tile_index == 0
    tile_rows = pivot_inverse.shape[1]

    def table(values):
        return jnp.asarray(np.array(values, dtype=bool))[position]

    own_role = [False] * steps
    for level_index, step_plan in levels_plan.items():
        for where_at in range(steps):
            if step_plan["active"][where_at]:
                own_role[where_at] = step_plan["c_left"][where_at]
    role = table(own_role)

    own_left = mult_left[0]
    own_right = mult_right[0]
    inverse_rows = pivot_inverse[0]
    full_left = join_tiles(own_left, is_first, axis=0)
    full_right = join_tiles(own_right, is_first, axis=0)
    full_tip = join_tiles(mult_tip[0], is_first, axis=0)
    first = jnp.where(role, full_left, full_right)
    second = jnp.where(role, full_right, full_left)
    stacked = jnp.concatenate([first, second, full_tip], axis=0)
    col_start = tile_index * tile_rows
    first_cols = lax.dynamic_slice_in_dim(first, col_start, tile_rows, 1)
    second_cols = lax.dynamic_slice_in_dim(second, col_start, tile_rows, 1)
    tip_cols = lax.dynamic_slice_in_dim(full_tip, col_start, tile_rows, 1)
    tip_own = product(root_tip, tip_cols)

    zero_rows = jnp.zeros_like(inverse_rows)
    zero_tip = jnp.zeros_like(root_cross)

    up_diag, up_tip, up_self_left, up_self_right = inverse_rows, root_cross, None, None
    state_diag, state_tip = inverse_rows, root_cross
    state_cross = jnp.zeros((tile_rows, 2 * inverse_rows.shape[1]), inverse_rows.dtype)
    history = {levels: (state_diag, state_tip)}

    for level_index in reversed(range(levels)):
        step_plan = levels_plan[level_index]
        active = table(step_plan["active"])

        from_left = send((up_diag, up_tip), step_plan["crit_from_left"])
        from_right = send((up_diag, up_tip), step_plan["crit_from_right"])
        near_diag = pick(role, *(None if r is None else r[0] for r in (from_left, from_right)))
        near_tip = pick(role, *(None if r is None else r[1] for r in (from_left, from_right)))
        if up_self_left is None:
            cross = None
        else:
            cross_left = send(up_self_right, step_plan["crit_from_left"])
            cross_right = send(up_self_left, step_plan["crit_from_right"])
            cross = pick(role, cross_left, cross_right)

        older = history.get(level_index + 2)
        far_diag, far_tip = zero_rows, zero_tip
        if older is not None:
            g_left = send(older, step_plan["pre_from_left"])
            g_right = send(older, step_plan["pre_from_right"])
            if g_left is not None or g_right is not None:
                far_diag = pick(role, *(None if r is None else r[0] for r in (g_right, g_left)))
                far_tip = pick(role, *(None if r is None else r[1] for r in (g_right, g_left)))

        tips_full = join_tiles(jnp.stack([near_tip, far_tip]), is_first)
        if cross is None:
            near_operand = jnp.concatenate([near_diag, near_tip.T], axis=1)
            near_mult = jnp.concatenate([first, full_tip], axis=0)
            far_operand = jnp.concatenate([far_diag, far_tip.T], axis=1)
            far_mult = jnp.concatenate([second, full_tip], axis=0)
        else:
            cross_turned = tile_transpose(cross[None], is_first)[0]
            near_operand = jnp.concatenate([near_diag, cross, near_tip.T], axis=1)
            near_mult = stacked
            far_operand = jnp.concatenate([cross_turned, far_diag, far_tip.T], axis=1)
            far_mult = stacked
        fresh_far = (-product(far_operand, far_mult)).astype(jnp.bfloat16)
        fresh_near = (-product(near_operand, near_mult)).astype(jnp.bfloat16)
        tip_y = product(tips_full[0], first_cols) + product(tips_full[1], second_cols) + tip_own
        fresh_tip = (-tip_y).astype(jnp.bfloat16)
        turned = tile_transpose(jnp.stack([fresh_near, fresh_far]), is_first)
        own_near = turned[0]
        own_far = turned[1]
        total = product(jnp.concatenate([own_near, own_far, fresh_tip.T], axis=1), stacked)
        fresh_diag = (inverse_rows.astype(jnp.float32) - total).astype(jnp.bfloat16)
        self_left = jnp.where(role, own_near, own_far)
        self_right = jnp.where(role, own_far, own_near)

        state_diag = jnp.where(active, fresh_diag, state_diag)
        state_tip = jnp.where(active, fresh_tip, state_tip)
        state_cross = jnp.where(active, jnp.concatenate([self_left, self_right], axis=1), state_cross)
        if level_index > 0:
            state_diag, state_tip, state_cross = lax.optimization_barrier((state_diag, state_tip, state_cross))
        history[level_index] = (state_diag, state_tip)
        up_diag, up_tip, up_self_left, up_self_right = fresh_diag, fresh_tip, self_left, self_right

    return (state_diag[None], state_cross[None], state_tip[None])


def solution(mesh):
    placed = (
        P("tm", "tile", None),
        P("tm", "tile", None),
        P("tm", "tile", None),
        P("tm", "tile", None),
        P(None, "tile"),
        P(),
    )
    return jax.shard_map(
        body,
        mesh=mesh,
        in_specs=placed,
        out_specs=(P("tm", "tile", None), P("tm", "tile", None), P("tm", None, "tile")),
        check_vma=False,
    )
```

```python
import numpy as np

import jax
import jax.numpy as jnp
from jax import lax
from jax.sharding import PartitionSpec as P


def product(left_matrix, right_matrix):
    return jnp.dot(left_matrix, right_matrix, preferred_element_type=jnp.float32)


def level_of(block, steps, levels):
    if block == steps - 1:
        return levels
    level = 0
    while (block >> level) & 1:
        level += 1
    return level


def plan(steps, levels, offset):
    where_is = lambda block: (block - offset) % steps
    levels_plan = {}
    for level_index in reversed(range(levels)):
        distance = 2**level_index
        crit_from_left, crit_from_right = [], []
        pre_from_left, pre_from_right = [], []
        c_left = [False] * steps
        active = [False] * steps
        for block in range(steps):
            if block % (2 * distance) != distance - 1:
                continue
            active[where_is(block)] = True
            left_id, right_id = block - distance, block + distance
            if left_id >= 0 and level_of(left_id, steps, levels) == level_index + 1:
                c_left[where_is(block)] = True
                crit_from_left.append((where_is(left_id), where_is(block)))
                pre_from_right.append((where_is(right_id), where_is(block)))
            else:
                crit_from_right.append((where_is(right_id), where_is(block)))
                if left_id >= 0:
                    pre_from_left.append((where_is(left_id), where_is(block)))
        relays = choose_relays(crit_from_left + crit_from_right, steps)
        levels_plan[level_index] = dict(
            crit_from_left=[pair for pair in crit_from_left if pair not in relays],
            crit_from_right=[pair for pair in crit_from_right if pair not in relays],
            leg_from_left=[(pair[0], relays[pair]) for pair in crit_from_left if pair in relays],
            leg_from_right=[(pair[0], relays[pair]) for pair in crit_from_right if pair in relays],
            leg_on=[(via, pair[1]) for pair, via in relays.items()],
            pre_from_left=pre_from_left,
            pre_from_right=pre_from_right,
            c_left=c_left,
            active=active,
        )
    return levels_plan


def ring_route(source, target, tie):
    here = [source % 4, (source // 4) % 4, source // 16]
    there = [target % 4, (target // 4) % 4, target // 16]
    links = []
    for dim in range(3):
        while here[dim] != there[dim]:
            gap = (there[dim] - here[dim]) % 4
            step = 1 if gap < 2 else (-1 if gap > 2 else tie)
            after = list(here)
            after[dim] = (here[dim] + step) % 4
            links.append((tuple(here), tuple(after)))
            here = after
    return links


def link_load(flows, relays):
    worst = (0, 0)
    for tie in (1, -1):
        load = {}
        for source, target in flows:
            via = relays.get((source, target))
            path = ring_route(source, target, tie) if via is None else (
                ring_route(source, via, tie) + ring_route(via, target, tie))
            for link in path:
                load[link] = load.get(link, 0) + 1
        top = max(load.values())
        worst = max(worst, (top, sum(1 for v in load.values() if v == top)))
    return worst


def choose_relays(flows, steps):
    relays = {}
    if steps != 64:
        return relays
    by_source = {}
    for source, target in flows:
        by_source.setdefault(source, []).append(target)
    for source, targets in sorted(by_source.items()):
        if len(targets) < 2:
            continue
        if not set(ring_route(source, targets[0], 1)) & set(ring_route(source, targets[1], 1)):
            continue
        best = (link_load(flows, relays), None)
        for target in targets:
            for dim in range(3):
                for step in (1, -1):
                    at = [source % 4, (source // 4) % 4, source // 16]
                    at[dim] = (at[dim] + step) % 4
                    via = at[0] + 4 * at[1] + 16 * at[2]
                    if via == target or via in relays.values():
                        continue
                    relays[(source, target)] = via
                    score = link_load(flows, relays)
                    del relays[(source, target)]
                    if score < best[0]:
                        best = (score, (source, target, via))
        if best[1] is not None:
            relays[best[1][:2]] = best[1][2]
    return relays


def pick(flag, if_true, if_false):
    if if_true is None:
        return if_false
    if if_false is None:
        return if_true
    return jnp.where(flag, if_true, if_false)


def add_present(first, second):
    if first is None:
        return second
    if second is None:
        return first
    return jax.tree.map(lambda a, b: a + b, first, second)


def send(values, pairs):
    if not pairs:
        return None
    return lax.ppermute(values, "tm", pairs)


def swap_tiles(values):
    return lax.ppermute(values, "tile", [(0, 1), (1, 0)])


def tile_transpose(blocks, is_first):
    half = blocks.shape[1]
    left, right = blocks[:, :, :half], blocks[:, :, half:]
    mine = jnp.where(is_first, left, right)
    got = swap_tiles(jnp.where(is_first, right, left))
    top = jnp.where(is_first, mine, got)
    bottom = jnp.where(is_first, got, mine)
    return jnp.concatenate([jnp.swapaxes(top, 1, 2), jnp.swapaxes(bottom, 1, 2)], axis=2)


def join_tiles(halves, is_first, axis=-1):
    got = swap_tiles(halves)
    return jnp.where(
        is_first, jnp.concatenate([halves, got], axis=axis), jnp.concatenate([got, halves], axis=axis)
    )


def body(pivot_inverse, mult_left, mult_right, mult_tip, root_cross, root_tip):
    steps = lax.axis_size("tm")
    levels = steps.bit_length() - 1
    offset = 5 % steps
    levels_plan = plan(steps, levels, offset)
    position = lax.axis_index("tm")
    tile_index = lax.axis_index("tile")
    is_first = tile_index == 0
    tile_rows = pivot_inverse.shape[1]

    def table(values):
        return jnp.asarray(np.array(values, dtype=bool))[position]

    own_role = [False] * steps
    for level_index, step_plan in levels_plan.items():
        for where_at in range(steps):
            if step_plan["active"][where_at]:
                own_role[where_at] = step_plan["c_left"][where_at]
    role = table(own_role)

    own_left = mult_left[0]
    own_right = mult_right[0]
    inverse_rows = pivot_inverse[0]
    full_left = join_tiles(own_left, is_first, axis=0)
    full_right = join_tiles(own_right, is_first, axis=0)
    full_tip = join_tiles(mult_tip[0], is_first, axis=0)
    first = jnp.where(role, full_left, full_right)
    second = jnp.where(role, full_right, full_left)
    stacked = jnp.concatenate([first, second, full_tip], axis=0)
    col_start = tile_index * tile_rows
    first_cols = lax.dynamic_slice_in_dim(first, col_start, tile_rows, 1)
    second_cols = lax.dynamic_slice_in_dim(second, col_start, tile_rows, 1)
    tip_cols = lax.dynamic_slice_in_dim(full_tip, col_start, tile_rows, 1)
    tip_own = product(root_tip, tip_cols)

    zero_rows = jnp.zeros_like(inverse_rows)
    zero_tip = jnp.zeros_like(root_cross)

    up_diag, up_tip, up_self_left, up_self_right = inverse_rows, root_cross, None, None
    state_diag, state_tip = inverse_rows, root_cross
    state_cross = jnp.zeros((tile_rows, 2 * inverse_rows.shape[1]), inverse_rows.dtype)
    history = {levels: (state_diag, state_tip)}

    for level_index in reversed(range(levels)):
        step_plan = levels_plan[level_index]
        active = table(step_plan["active"])

        from_left = send((up_diag, up_tip), step_plan["crit_from_left"])
        from_right = send((up_diag, up_tip), step_plan["crit_from_right"])
        near_diag = pick(role, *(None if r is None else r[0] for r in (from_left, from_right)))
        near_tip = pick(role, *(None if r is None else r[1] for r in (from_left, from_right)))
        relayed = None
        if step_plan["leg_on"]:
            leg_left = send((up_diag, up_tip), step_plan["leg_from_left"])
            leg_right = send((up_diag, up_tip), step_plan["leg_from_right"])
            held = add_present(leg_left, leg_right)
            relayed = send(held, step_plan["leg_on"])
            near_diag = add_present(near_diag, relayed[0])
            near_tip = add_present(near_tip, relayed[1])
        if up_self_left is None:
            cross = None
        else:
            cross_left = send(up_self_right, step_plan["crit_from_left"])
            cross_right = send(up_self_left, step_plan["crit_from_right"])
            cross = pick(role, cross_left, cross_right)
            if relayed is not None:
                held_cross = add_present(
                    send(up_self_right, step_plan["leg_from_left"]), send(up_self_left, step_plan["leg_from_right"])
                )
                cross = add_present(cross, send(held_cross, step_plan["leg_on"]))

        older = history.get(level_index + 2)
        far_diag, far_tip = zero_rows, zero_tip
        if older is not None:
            g_left = send(older, step_plan["pre_from_left"])
            g_right = send(older, step_plan["pre_from_right"])
            if g_left is not None or g_right is not None:
                far_diag = pick(role, *(None if r is None else r[0] for r in (g_right, g_left)))
                far_tip = pick(role, *(None if r is None else r[1] for r in (g_right, g_left)))

        tips_full = join_tiles(jnp.stack([near_tip, far_tip]), is_first)
        if cross is None:
            near_operand = jnp.concatenate([near_diag, near_tip.T], axis=1)
            near_mult = jnp.concatenate([first, full_tip], axis=0)
            far_operand = jnp.concatenate([far_diag, far_tip.T], axis=1)
            far_mult = jnp.concatenate([second, full_tip], axis=0)
        else:
            cross_turned = tile_transpose(cross[None], is_first)[0]
            near_operand = jnp.concatenate([near_diag, cross, near_tip.T], axis=1)
            near_mult = stacked
            far_operand = jnp.concatenate([cross_turned, far_diag, far_tip.T], axis=1)
            far_mult = stacked
        fresh_far = (-product(far_operand, far_mult)).astype(jnp.bfloat16)
        fresh_near = (-product(near_operand, near_mult)).astype(jnp.bfloat16)
        tip_y = product(tips_full[0], first_cols) + product(tips_full[1], second_cols) + tip_own
        fresh_tip = (-tip_y).astype(jnp.bfloat16)
        turned = tile_transpose(jnp.stack([fresh_near, fresh_far]), is_first)
        own_near = turned[0]
        own_far = turned[1]
        total = product(jnp.concatenate([own_near, own_far, fresh_tip.T], axis=1), stacked)
        fresh_diag = (inverse_rows.astype(jnp.float32) - total).astype(jnp.bfloat16)
        self_left = jnp.where(role, own_near, own_far)
        self_right = jnp.where(role, own_far, own_near)

        state_diag = jnp.where(active, fresh_diag, state_diag)
        state_tip = jnp.where(active, fresh_tip, state_tip)
        state_cross = jnp.where(active, jnp.concatenate([self_left, self_right], axis=1), state_cross)
        if level_index > 0:
            state_diag, state_tip, state_cross = lax.optimization_barrier((state_diag, state_tip, state_cross))
        history[level_index] = (state_diag, state_tip)
        up_diag, up_tip, up_self_left, up_self_right = fresh_diag, fresh_tip, self_left, self_right

    return (state_diag[None], state_cross[None], state_tip[None])


def solution(mesh):
    placed = (
        P("tm", "tile", None),
        P("tm", "tile", None),
        P("tm", "tile", None),
        P("tm", "tile", None),
        P(None, "tile"),
        P(),
    )
    return jax.shard_map(
        body,
        mesh=mesh,
        in_specs=placed,
        out_specs=(P("tm", "tile", None), P("tm", "tile", None), P("tm", None, "tile")),
        check_vma=False,
    )
```

```python
import numpy as np

import jax
import jax.numpy as jnp
from jax import lax
from jax.sharding import PartitionSpec as P


def product(left_matrix, right_matrix):
    return jnp.dot(left_matrix, right_matrix, preferred_element_type=jnp.float32)


def level_of(block, steps, levels):
    if block == steps - 1:
        return levels
    level = 0
    while (block >> level) & 1:
        level += 1
    return level


def plan(steps, levels, offset):
    where_is = lambda block: (block - offset) % steps
    levels_plan = {}
    for level_index in reversed(range(levels)):
        distance = 2**level_index
        crit_from_left, crit_from_right = [], []
        pre_from_left, pre_from_right = [], []
        c_left = [False] * steps
        active = [False] * steps
        for block in range(steps):
            if block % (2 * distance) != distance - 1:
                continue
            active[where_is(block)] = True
            left_id, right_id = block - distance, block + distance
            if left_id >= 0 and level_of(left_id, steps, levels) == level_index + 1:
                c_left[where_is(block)] = True
                crit_from_left.append((where_is(left_id), where_is(block)))
                pre_from_right.append((where_is(right_id), where_is(block)))
            else:
                crit_from_right.append((where_is(right_id), where_is(block)))
                if left_id >= 0:
                    pre_from_left.append((where_is(left_id), where_is(block)))
        relays = choose_relays(crit_from_left + crit_from_right, steps)
        levels_plan[level_index] = dict(
            crit_from_left=[pair for pair in crit_from_left if pair not in relays],
            crit_from_right=[pair for pair in crit_from_right if pair not in relays],
            leg_from_left=[(pair[0], relays[pair]) for pair in crit_from_left if pair in relays],
            leg_from_right=[(pair[0], relays[pair]) for pair in crit_from_right if pair in relays],
            leg_on=[(via, pair[1]) for pair, via in relays.items()],
            pre_from_left=pre_from_left,
            pre_from_right=pre_from_right,
            c_left=c_left,
            active=active,
        )
    return levels_plan


def ring_route(source, target, tie):
    here = [source % 4, (source // 4) % 4, source // 16]
    there = [target % 4, (target // 4) % 4, target // 16]
    links = []
    for dim in range(3):
        while here[dim] != there[dim]:
            gap = (there[dim] - here[dim]) % 4
            step = 1 if gap < 2 else (-1 if gap > 2 else tie)
            after = list(here)
            after[dim] = (here[dim] + step) % 4
            links.append((tuple(here), tuple(after)))
            here = after
    return links


def link_load(flows, relays):
    worst = (0, 0)
    for tie in (1, -1):
        load = {}
        for source, target in flows:
            via = relays.get((source, target))
            path = ring_route(source, target, tie) if via is None else (
                ring_route(source, via, tie) + ring_route(via, target, tie))
            for link in path:
                load[link] = load.get(link, 0) + 1
        top = max(load.values())
        worst = max(worst, (top, sum(1 for v in load.values() if v == top)))
    return worst


def choose_relays(flows, steps):
    relays = {}
    if steps != 64:
        return relays
    by_source = {}
    for source, target in flows:
        by_source.setdefault(source, []).append(target)
    for source, targets in sorted(by_source.items()):
        if len(targets) < 2:
            continue
        if not set(ring_route(source, targets[0], 1)) & set(ring_route(source, targets[1], 1)):
            continue
        best = (link_load(flows, relays), None)
        for target in targets:
            for dim in range(3):
                for step in (1, -1):
                    at = [source % 4, (source // 4) % 4, source // 16]
                    at[dim] = (at[dim] + step) % 4
                    via = at[0] + 4 * at[1] + 16 * at[2]
                    if via == target or via in relays.values():
                        continue
                    relays[(source, target)] = via
                    score = link_load(flows, relays)
                    del relays[(source, target)]
                    if score < best[0]:
                        best = (score, (source, target, via))
        if best[1] is not None:
            relays[best[1][:2]] = best[1][2]
    return relays


def pick(flag, if_true, if_false):
    if if_true is None:
        return if_false
    if if_false is None:
        return if_true
    return jnp.where(flag, if_true, if_false)


def add_present(first, second):
    if first is None:
        return second
    if second is None:
        return first
    return jax.tree.map(lambda a, b: a + b, first, second)


def send(values, pairs):
    if not pairs:
        return None
    return lax.ppermute(values, "tm", pairs)


def swap_tiles(values):
    return lax.ppermute(values, "tile", [(0, 1), (1, 0)])


def tile_transpose(blocks, is_first):
    half = blocks.shape[1]
    left, right = blocks[:, :, :half], blocks[:, :, half:]
    mine = jnp.where(is_first, left, right)
    got = swap_tiles(jnp.where(is_first, right, left))
    top = jnp.where(is_first, mine, got)
    bottom = jnp.where(is_first, got, mine)
    return jnp.concatenate([jnp.swapaxes(top, 1, 2), jnp.swapaxes(bottom, 1, 2)], axis=2)


def join_tiles(halves, is_first, axis=-1):
    got = swap_tiles(halves)
    return jnp.where(
        is_first, jnp.concatenate([halves, got], axis=axis), jnp.concatenate([got, halves], axis=axis)
    )


def body(pivot_inverse, mult_left, mult_right, mult_tip, root_cross, root_tip):
    steps = lax.axis_size("tm")
    levels = steps.bit_length() - 1
    offset = 5 % steps
    levels_plan = plan(steps, levels, offset)
    position = lax.axis_index("tm")
    tile_index = lax.axis_index("tile")
    is_first = tile_index == 0
    tile_rows = pivot_inverse.shape[1]

    def table(values):
        return jnp.asarray(np.array(values, dtype=bool))[position]

    own_role = [False] * steps
    for level_index, step_plan in levels_plan.items():
        for where_at in range(steps):
            if step_plan["active"][where_at]:
                own_role[where_at] = step_plan["c_left"][where_at]
    role = table(own_role)

    own_left = mult_left[0]
    own_right = mult_right[0]
    inverse_rows = pivot_inverse[0]
    full_left = join_tiles(own_left, is_first, axis=0)
    full_right = join_tiles(own_right, is_first, axis=0)
    full_tip = join_tiles(mult_tip[0], is_first, axis=0)
    first = jnp.where(role, full_left, full_right)
    second = jnp.where(role, full_right, full_left)
    stacked = jnp.concatenate([first, second, full_tip], axis=0)
    col_start = tile_index * tile_rows
    first_cols = lax.dynamic_slice_in_dim(first, col_start, tile_rows, 1)
    second_cols = lax.dynamic_slice_in_dim(second, col_start, tile_rows, 1)
    tip_cols = lax.dynamic_slice_in_dim(full_tip, col_start, tile_rows, 1)
    tip_own = product(root_tip, tip_cols)

    zero_rows = jnp.zeros_like(inverse_rows)
    zero_tip = jnp.zeros_like(root_cross)

    nodes = inverse_rows.shape[1]
    top_pack = jnp.concatenate([inverse_rows, root_cross.T], axis=1)
    pack_left, pack_right, has_cross = top_pack, top_pack, False
    state_diag, state_tip = inverse_rows, root_cross
    state_cross = jnp.zeros((tile_rows, 2 * nodes), inverse_rows.dtype)
    history = {levels: (state_diag, state_tip)}

    for level_index in reversed(range(levels)):
        step_plan = levels_plan[level_index]
        active = table(step_plan["active"])

        near = pick(
            role, send(pack_right, step_plan["crit_from_left"]), send(pack_left, step_plan["crit_from_right"])
        )
        if step_plan["leg_on"]:
            held = add_present(
                send(pack_right, step_plan["leg_from_left"]), send(pack_left, step_plan["leg_from_right"])
            )
            near = add_present(near, send(held, step_plan["leg_on"]))
        near_tip = near[:, -root_cross.shape[0]:].T

        older = history.get(level_index + 2)
        far = None
        if older is not None:
            older_pack = jnp.concatenate([older[0], older[1].T], axis=1)
            far = pick(
                role, send(older_pack, step_plan["pre_from_right"]), send(older_pack, step_plan["pre_from_left"])
            )
        if far is None:
            far = jnp.zeros((tile_rows, nodes + root_cross.shape[0]), inverse_rows.dtype)
        far_tip = far[:, nodes:].T

        tips_full = join_tiles(jnp.stack([near_tip, far_tip]), is_first)
        near_operand = near
        if has_cross:
            cross_turned = tile_transpose(near[:, nodes:2 * nodes][None], is_first)[0]
            near_mult = stacked
            far_operand = jnp.concatenate([cross_turned, far], axis=1)
            far_mult = stacked
        else:
            near_mult = jnp.concatenate([first, full_tip], axis=0)
            far_operand = far
            far_mult = jnp.concatenate([second, full_tip], axis=0)
        fresh_far = (-product(far_operand, far_mult)).astype(jnp.bfloat16)
        fresh_near = (-product(near_operand, near_mult)).astype(jnp.bfloat16)
        tip_y = product(tips_full[0], first_cols) + product(tips_full[1], second_cols) + tip_own
        fresh_tip = (-tip_y).astype(jnp.bfloat16)
        turned = tile_transpose(jnp.stack([fresh_near, fresh_far]), is_first)
        own_near = turned[0]
        own_far = turned[1]
        total = product(jnp.concatenate([own_near, own_far, fresh_tip.T], axis=1), stacked)
        fresh_diag = (inverse_rows.astype(jnp.float32) - total).astype(jnp.bfloat16)
        self_left = jnp.where(role, own_near, own_far)
        self_right = jnp.where(role, own_far, own_near)

        state_diag = jnp.where(active, fresh_diag, state_diag)
        state_tip = jnp.where(active, fresh_tip, state_tip)
        state_cross = jnp.where(active, jnp.concatenate([self_left, self_right], axis=1), state_cross)
        if level_index > 0:
            state_diag, state_tip, state_cross = lax.optimization_barrier((state_diag, state_tip, state_cross))
        history[level_index] = (state_diag, state_tip)
        pack_left = jnp.concatenate([fresh_diag, self_left, fresh_tip.T], axis=1)
        pack_right = jnp.concatenate([fresh_diag, self_right, fresh_tip.T], axis=1)
        has_cross = True

    return (state_diag[None], state_cross[None], state_tip[None])


def solution(mesh):
    placed = (
        P("tm", "tile", None),
        P("tm", "tile", None),
        P("tm", "tile", None),
        P("tm", "tile", None),
        P(None, "tile"),
        P(),
    )
    return jax.shard_map(
        body,
        mesh=mesh,
        in_specs=placed,
        out_specs=(P("tm", "tile", None), P("tm", "tile", None), P("tm", None, "tile")),
        check_vma=False,
    )
```

```python
import numpy as np

import jax
import jax.numpy as jnp
from jax import lax
from jax.sharding import PartitionSpec as P


def product(left_matrix, right_matrix):
    return jnp.dot(left_matrix, right_matrix, preferred_element_type=jnp.float32)


def level_of(block, steps, levels):
    if block == steps - 1:
        return levels
    level = 0
    while (block >> level) & 1:
        level += 1
    return level


def plan(steps, levels, offset):
    where_is = lambda block: (block - offset) % steps
    levels_plan = {}
    for level_index in reversed(range(levels)):
        distance = 2**level_index
        crit_from_left, crit_from_right = [], []
        pre_from_left, pre_from_right = [], []
        c_left = [False] * steps
        active = [False] * steps
        for block in range(steps):
            if block % (2 * distance) != distance - 1:
                continue
            active[where_is(block)] = True
            left_id, right_id = block - distance, block + distance
            if left_id >= 0 and level_of(left_id, steps, levels) == level_index + 1:
                c_left[where_is(block)] = True
                crit_from_left.append((where_is(left_id), where_is(block)))
                pre_from_right.append((where_is(right_id), where_is(block)))
            else:
                crit_from_right.append((where_is(right_id), where_is(block)))
                if left_id >= 0:
                    pre_from_left.append((where_is(left_id), where_is(block)))
        relays = choose_relays(crit_from_left + crit_from_right, steps)
        levels_plan[level_index] = dict(
            crit_from_left=[pair for pair in crit_from_left if pair not in relays],
            crit_from_right=[pair for pair in crit_from_right if pair not in relays],
            leg_from_left=[(pair[0], relays[pair]) for pair in crit_from_left if pair in relays],
            leg_from_right=[(pair[0], relays[pair]) for pair in crit_from_right if pair in relays],
            leg_on=[(via, pair[1]) for pair, via in relays.items()],
            pre_from_left=pre_from_left,
            pre_from_right=pre_from_right,
            c_left=c_left,
            active=active,
        )
    return levels_plan


def ring_route(source, target, tie):
    here = [source % 4, (source // 4) % 4, source // 16]
    there = [target % 4, (target // 4) % 4, target // 16]
    links = []
    for dim in range(3):
        while here[dim] != there[dim]:
            gap = (there[dim] - here[dim]) % 4
            step = 1 if gap < 2 else (-1 if gap > 2 else tie)
            after = list(here)
            after[dim] = (here[dim] + step) % 4
            links.append((tuple(here), tuple(after)))
            here = after
    return links


def link_load(flows, relays):
    worst = (0, 0)
    for tie in (1, -1):
        load = {}
        for source, target in flows:
            via = relays.get((source, target))
            path = ring_route(source, target, tie) if via is None else (
                ring_route(source, via, tie) + ring_route(via, target, tie))
            for link in path:
                load[link] = load.get(link, 0) + 1
        top = max(load.values())
        worst = max(worst, (top, sum(1 for v in load.values() if v == top)))
    return worst


def choose_relays(flows, steps):
    relays = {}
    if steps != 64:
        return relays
    by_source = {}
    for source, target in flows:
        by_source.setdefault(source, []).append(target)
    for source, targets in sorted(by_source.items()):
        if len(targets) < 2:
            continue
        if not set(ring_route(source, targets[0], 1)) & set(ring_route(source, targets[1], 1)):
            continue
        best = (link_load(flows, relays), None)
        for target in targets:
            for dim in range(3):
                for step in (1, -1):
                    at = [source % 4, (source // 4) % 4, source // 16]
                    at[dim] = (at[dim] + step) % 4
                    via = at[0] + 4 * at[1] + 16 * at[2]
                    if via == target or via in relays.values():
                        continue
                    relays[(source, target)] = via
                    score = link_load(flows, relays)
                    del relays[(source, target)]
                    if score < best[0]:
                        best = (score, (source, target, via))
        if best[1] is not None:
            relays[best[1][:2]] = best[1][2]
    return relays


def pick(flag, if_true, if_false):
    if if_true is None:
        return if_false
    if if_false is None:
        return if_true
    return jnp.where(flag, if_true, if_false)


def add_present(first, second):
    if first is None:
        return second
    if second is None:
        return first
    return jax.tree.map(lambda a, b: a + b, first, second)


def send(values, pairs):
    if not pairs:
        return None
    return lax.ppermute(values, "tm", pairs)


def swap_tiles(values):
    return lax.ppermute(values, "tile", [(0, 1), (1, 0)])


def tile_transpose(blocks, is_first):
    half = blocks.shape[1]
    left, right = blocks[:, :, :half], blocks[:, :, half:]
    mine = jnp.where(is_first, left, right)
    got = swap_tiles(jnp.where(is_first, right, left))
    top = jnp.where(is_first, mine, got)
    bottom = jnp.where(is_first, got, mine)
    return jnp.concatenate([jnp.swapaxes(top, 1, 2), jnp.swapaxes(bottom, 1, 2)], axis=2)


def join_tiles(halves, is_first, axis=-1):
    got = swap_tiles(halves)
    return jnp.where(
        is_first, jnp.concatenate([halves, got], axis=axis), jnp.concatenate([got, halves], axis=axis)
    )


def body(pivot_inverse, mult_left, mult_right, mult_tip, root_cross, root_tip):
    steps = lax.axis_size("tm")
    levels = steps.bit_length() - 1
    offset = 5 % steps
    levels_plan = plan(steps, levels, offset)
    position = lax.axis_index("tm")
    tile_index = lax.axis_index("tile")
    is_first = tile_index == 0
    tile_rows = pivot_inverse.shape[1]

    def table(values):
        return jnp.asarray(np.array(values, dtype=bool))[position]

    own_role = [False] * steps
    for level_index, step_plan in levels_plan.items():
        for where_at in range(steps):
            if step_plan["active"][where_at]:
                own_role[where_at] = step_plan["c_left"][where_at]
    role = table(own_role)

    own_left = mult_left[0]
    own_right = mult_right[0]
    inverse_rows = pivot_inverse[0]
    full_left = join_tiles(own_left, is_first, axis=0)
    full_right = join_tiles(own_right, is_first, axis=0)
    full_tip = join_tiles(mult_tip[0], is_first, axis=0)
    first = jnp.where(role, full_left, full_right)
    second = jnp.where(role, full_right, full_left)
    stacked = jnp.concatenate([first, second, full_tip], axis=0)
    col_start = tile_index * tile_rows
    first_cols = lax.dynamic_slice_in_dim(first, col_start, tile_rows, 1)
    second_cols = lax.dynamic_slice_in_dim(second, col_start, tile_rows, 1)
    tip_cols = lax.dynamic_slice_in_dim(full_tip, col_start, tile_rows, 1)
    tip_own = product(root_tip, tip_cols)

    zero_rows = jnp.zeros_like(inverse_rows)
    zero_tip = jnp.zeros_like(root_cross)

    up_diag, up_tip, up_self_left, up_self_right = inverse_rows, root_cross, None, None
    state_diag, state_tip = inverse_rows, root_cross
    state_cross = jnp.zeros((tile_rows, 2 * inverse_rows.shape[1]), inverse_rows.dtype)
    history = {levels: (state_diag, state_tip)}

    for level_index in reversed(range(levels)):
        step_plan = levels_plan[level_index]
        active = table(step_plan["active"])

        def arrive(right_going, left_going):
            got = pick(role, send(right_going, step_plan["crit_from_left"]), send(left_going, step_plan["crit_from_right"]))
            if step_plan["leg_on"]:
                held = add_present(
                    send(right_going, step_plan["leg_from_left"]), send(left_going, step_plan["leg_from_right"])
                )
                got = add_present(got, send(held, step_plan["leg_on"]))
            return got

        near_diag = arrive(up_diag, up_diag)
        if up_self_left is None:
            cross = None
            near_tip = arrive(up_tip, up_tip)
        else:
            early = arrive(
                jnp.concatenate([up_self_right, up_tip.T], axis=1), jnp.concatenate([up_self_left, up_tip.T], axis=1)
            )
            cross = early[:, : inverse_rows.shape[1]]
            near_tip = early[:, inverse_rows.shape[1]:].T

        older = history.get(level_index + 2)
        far_diag, far_tip = zero_rows, zero_tip
        if older is not None:
            g_left = send(older, step_plan["pre_from_left"])
            g_right = send(older, step_plan["pre_from_right"])
            if g_left is not None or g_right is not None:
                far_diag = pick(role, *(None if r is None else r[0] for r in (g_right, g_left)))
                far_tip = pick(role, *(None if r is None else r[1] for r in (g_right, g_left)))

        tips_full = join_tiles(jnp.stack([near_tip, far_tip]), is_first)
        if cross is None:
            near_operand = jnp.concatenate([near_diag, near_tip.T], axis=1)
            near_mult = jnp.concatenate([first, full_tip], axis=0)
            far_operand = jnp.concatenate([far_diag, far_tip.T], axis=1)
            far_mult = jnp.concatenate([second, full_tip], axis=0)
        else:
            cross_turned = tile_transpose(cross[None], is_first)[0]
            near_operand = jnp.concatenate([near_diag, cross, near_tip.T], axis=1)
            near_mult = stacked
            far_operand = jnp.concatenate([cross_turned, far_diag, far_tip.T], axis=1)
            far_mult = stacked
        fresh_far = (-product(far_operand, far_mult)).astype(jnp.bfloat16)
        fresh_near = (-product(near_operand, near_mult)).astype(jnp.bfloat16)
        tip_y = product(tips_full[0], first_cols) + product(tips_full[1], second_cols) + tip_own
        fresh_tip = (-tip_y).astype(jnp.bfloat16)
        turned = tile_transpose(jnp.stack([fresh_near, fresh_far]), is_first)
        own_near = turned[0]
        own_far = turned[1]
        total = product(jnp.concatenate([own_near, own_far, fresh_tip.T], axis=1), stacked)
        fresh_diag = (inverse_rows.astype(jnp.float32) - total).astype(jnp.bfloat16)
        self_left = jnp.where(role, own_near, own_far)
        self_right = jnp.where(role, own_far, own_near)

        state_diag = jnp.where(active, fresh_diag, state_diag)
        state_tip = jnp.where(active, fresh_tip, state_tip)
        state_cross = jnp.where(active, jnp.concatenate([self_left, self_right], axis=1), state_cross)
        if level_index > 0:
            state_diag, state_tip, state_cross = lax.optimization_barrier((state_diag, state_tip, state_cross))
        history[level_index] = (state_diag, state_tip)
        up_diag, up_tip, up_self_left, up_self_right = fresh_diag, fresh_tip, self_left, self_right

    return (state_diag[None], state_cross[None], state_tip[None])


def solution(mesh):
    placed = (
        P("tm", "tile", None),
        P("tm", "tile", None),
        P("tm", "tile", None),
        P("tm", "tile", None),
        P(None, "tile"),
        P(),
    )
    return jax.shard_map(
        body,
        mesh=mesh,
        in_specs=placed,
        out_specs=(P("tm", "tile", None), P("tm", "tile", None), P("tm", None, "tile")),
        check_vma=False,
    )
```

```python
import numpy as np

import jax
import jax.numpy as jnp
from jax import lax
from jax.sharding import PartitionSpec as P


def product(left_matrix, right_matrix):
    return jnp.dot(left_matrix, right_matrix, preferred_element_type=jnp.float32)


def level_of(block, steps, levels):
    if block == steps - 1:
        return levels
    level = 0
    while (block >> level) & 1:
        level += 1
    return level


def plan(steps, levels, offset):
    where_is = lambda block: (block - offset) % steps
    levels_plan = {}
    for level_index in reversed(range(levels)):
        distance = 2**level_index
        crit_from_left, crit_from_right = [], []
        pre_from_left, pre_from_right = [], []
        c_left = [False] * steps
        active = [False] * steps
        for block in range(steps):
            if block % (2 * distance) != distance - 1:
                continue
            active[where_is(block)] = True
            left_id, right_id = block - distance, block + distance
            if left_id >= 0 and level_of(left_id, steps, levels) == level_index + 1:
                c_left[where_is(block)] = True
                crit_from_left.append((where_is(left_id), where_is(block)))
                pre_from_right.append((where_is(right_id), where_is(block)))
            else:
                crit_from_right.append((where_is(right_id), where_is(block)))
                if left_id >= 0:
                    pre_from_left.append((where_is(left_id), where_is(block)))
        relays = choose_relays(crit_from_left + crit_from_right, steps)
        levels_plan[level_index] = dict(
            crit_from_left=[pair for pair in crit_from_left if pair not in relays],
            crit_from_right=[pair for pair in crit_from_right if pair not in relays],
            leg_from_left=[(pair[0], relays[pair]) for pair in crit_from_left if pair in relays],
            leg_from_right=[(pair[0], relays[pair]) for pair in crit_from_right if pair in relays],
            leg_on=[(via, pair[1]) for pair, via in relays.items()],
            pre_from_left=pre_from_left,
            pre_from_right=pre_from_right,
            c_left=c_left,
            active=active,
        )
    return levels_plan


def ring_route(source, target, tie):
    here = [source % 4, (source // 4) % 4, source // 16]
    there = [target % 4, (target // 4) % 4, target // 16]
    links = []
    for dim in range(3):
        while here[dim] != there[dim]:
            gap = (there[dim] - here[dim]) % 4
            step = 1 if gap < 2 else (-1 if gap > 2 else tie)
            after = list(here)
            after[dim] = (here[dim] + step) % 4
            links.append((tuple(here), tuple(after)))
            here = after
    return links


def link_load(flows, relays):
    worst = (0, 0)
    for tie in (1, -1):
        load = {}
        for source, target in flows:
            via = relays.get((source, target))
            path = ring_route(source, target, tie) if via is None else (
                ring_route(source, via, tie) + ring_route(via, target, tie))
            for link in path:
                load[link] = load.get(link, 0) + 1
        top = max(load.values())
        worst = max(worst, (top, sum(1 for v in load.values() if v == top)))
    return worst


def choose_relays(flows, steps):
    relays = {}
    if steps != 64:
        return relays
    by_source = {}
    for source, target in flows:
        by_source.setdefault(source, []).append(target)
    for source, targets in sorted(by_source.items()):
        if len(targets) < 2:
            continue
        if not set(ring_route(source, targets[0], 1)) & set(ring_route(source, targets[1], 1)):
            continue
        best = (link_load(flows, relays), None)
        for target in targets:
            for dim in range(3):
                for step in (1, -1):
                    at = [source % 4, (source // 4) % 4, source // 16]
                    at[dim] = (at[dim] + step) % 4
                    via = at[0] + 4 * at[1] + 16 * at[2]
                    if via == target or via in relays.values():
                        continue
                    relays[(source, target)] = via
                    score = link_load(flows, relays)
                    del relays[(source, target)]
                    if score < best[0]:
                        best = (score, (source, target, via))
        if best[1] is not None:
            relays[best[1][:2]] = best[1][2]
    return relays


def pick(flag, if_true, if_false):
    if if_true is None:
        return if_false
    if if_false is None:
        return if_true
    return jnp.where(flag, if_true, if_false)


def add_present(first, second):
    if first is None:
        return second
    if second is None:
        return first
    return jax.tree.map(lambda a, b: a + b, first, second)


def send(values, pairs):
    if not pairs:
        return None
    return lax.ppermute(values, "tm", pairs)


def swap_tiles(values):
    return lax.ppermute(values, "tile", [(0, 1), (1, 0)])


def tile_transpose(blocks, is_first):
    half = blocks.shape[1]
    left, right = blocks[:, :, :half], blocks[:, :, half:]
    mine = jnp.where(is_first, left, right)
    got = swap_tiles(jnp.where(is_first, right, left))
    top = jnp.where(is_first, mine, got)
    bottom = jnp.where(is_first, got, mine)
    return jnp.concatenate([jnp.swapaxes(top, 1, 2), jnp.swapaxes(bottom, 1, 2)], axis=2)


def join_tiles(halves, is_first, axis=-1):
    got = swap_tiles(halves)
    return jnp.where(
        is_first, jnp.concatenate([halves, got], axis=axis), jnp.concatenate([got, halves], axis=axis)
    )


def body(pivot_inverse, mult_left, mult_right, mult_tip, root_cross, root_tip):
    steps = lax.axis_size("tm")
    levels = steps.bit_length() - 1
    offset = 5 % steps
    levels_plan = plan(steps, levels, offset)
    position = lax.axis_index("tm")
    tile_index = lax.axis_index("tile")
    is_first = tile_index == 0
    tile_rows = pivot_inverse.shape[1]

    def table(values):
        return jnp.asarray(np.array(values, dtype=bool))[position]

    own_role = [False] * steps
    for level_index, step_plan in levels_plan.items():
        for where_at in range(steps):
            if step_plan["active"][where_at]:
                own_role[where_at] = step_plan["c_left"][where_at]
    role = table(own_role)

    own_left = mult_left[0]
    own_right = mult_right[0]
    inverse_rows = pivot_inverse[0]
    full_left = join_tiles(own_left, is_first, axis=0)
    full_right = join_tiles(own_right, is_first, axis=0)
    full_tip = join_tiles(mult_tip[0], is_first, axis=0)
    first = jnp.where(role, full_left, full_right)
    second = jnp.where(role, full_right, full_left)
    stacked = jnp.concatenate([first, second, full_tip], axis=0)
    col_start = tile_index * tile_rows
    first_cols = lax.dynamic_slice_in_dim(first, col_start, tile_rows, 1)
    second_cols = lax.dynamic_slice_in_dim(second, col_start, tile_rows, 1)
    tip_cols = lax.dynamic_slice_in_dim(full_tip, col_start, tile_rows, 1)
    tip_own = product(root_tip, tip_cols)

    zero_rows = jnp.zeros_like(inverse_rows)
    zero_tip = jnp.zeros_like(root_cross)

    up_diag, up_tip, up_self_left, up_self_right = inverse_rows, root_cross, None, None
    state_diag, state_tip = inverse_rows, root_cross
    state_cross = jnp.zeros((tile_rows, 2 * inverse_rows.shape[1]), inverse_rows.dtype)
    history = {levels: (state_diag, state_tip)}

    for level_index in reversed(range(levels)):
        step_plan = levels_plan[level_index]
        active = table(step_plan["active"])

        from_left = send((up_diag, up_tip), step_plan["crit_from_left"])
        from_right = send((up_diag, up_tip), step_plan["crit_from_right"])
        near_diag = pick(role, *(None if r is None else r[0] for r in (from_left, from_right)))
        near_tip = pick(role, *(None if r is None else r[1] for r in (from_left, from_right)))
        relayed = None
        if step_plan["leg_on"]:
            leg_left = send((up_diag, up_tip), step_plan["leg_from_left"])
            leg_right = send((up_diag, up_tip), step_plan["leg_from_right"])
            held = add_present(leg_left, leg_right)
            relayed = send(held, step_plan["leg_on"])
            near_diag = add_present(near_diag, relayed[0])
            near_tip = add_present(near_tip, relayed[1])
        if up_self_left is None:
            cross = None
        else:
            cross_left = send(up_self_right, step_plan["crit_from_left"])
            cross_right = send(up_self_left, step_plan["crit_from_right"])
            cross = pick(role, cross_left, cross_right)
            if relayed is not None:
                held_cross = add_present(
                    send(up_self_right, step_plan["leg_from_left"]), send(up_self_left, step_plan["leg_from_right"])
                )
                cross = add_present(cross, send(held_cross, step_plan["leg_on"]))

        older = history.get(level_index + 1)
        far_diag, far_tip = zero_rows, zero_tip
        if older is not None:
            g_left = send(older, step_plan["pre_from_left"])
            g_right = send(older, step_plan["pre_from_right"])
            if g_left is not None or g_right is not None:
                far_diag = pick(role, *(None if r is None else r[0] for r in (g_right, g_left)))
                far_tip = pick(role, *(None if r is None else r[1] for r in (g_right, g_left)))

        tips_full = join_tiles(jnp.stack([near_tip, far_tip]), is_first)
        if cross is None:
            near_operand = jnp.concatenate([near_diag, near_tip.T], axis=1)
            near_mult = jnp.concatenate([first, full_tip], axis=0)
            far_operand = jnp.concatenate([far_diag, far_tip.T], axis=1)
            far_mult = jnp.concatenate([second, full_tip], axis=0)
        else:
            cross_turned = tile_transpose(cross[None], is_first)[0]
            near_operand = jnp.concatenate([near_diag, cross, near_tip.T], axis=1)
            near_mult = stacked
            far_operand = jnp.concatenate([cross_turned, far_diag, far_tip.T], axis=1)
            far_mult = stacked
        fresh_far = (-product(far_operand, far_mult)).astype(jnp.bfloat16)
        fresh_near = (-product(near_operand, near_mult)).astype(jnp.bfloat16)
        tip_y = product(tips_full[0], first_cols) + product(tips_full[1], second_cols) + tip_own
        fresh_tip = (-tip_y).astype(jnp.bfloat16)
        turned = tile_transpose(jnp.stack([fresh_near, fresh_far]), is_first)
        own_near = turned[0]
        own_far = turned[1]
        total = product(jnp.concatenate([own_near, own_far, fresh_tip.T], axis=1), stacked)
        fresh_diag = (inverse_rows.astype(jnp.float32) - total).astype(jnp.bfloat16)
        self_left = jnp.where(role, own_near, own_far)
        self_right = jnp.where(role, own_far, own_near)

        state_diag = jnp.where(active, fresh_diag, state_diag)
        state_tip = jnp.where(active, fresh_tip, state_tip)
        state_cross = jnp.where(active, jnp.concatenate([self_left, self_right], axis=1), state_cross)
        if level_index > 0:
            state_diag, state_tip, state_cross = lax.optimization_barrier((state_diag, state_tip, state_cross))
        history[level_index] = (state_diag, state_tip)
        up_diag, up_tip, up_self_left, up_self_right = fresh_diag, fresh_tip, self_left, self_right

    return (state_diag[None], state_cross[None], state_tip[None])


def solution(mesh):
    placed = (
        P("tm", "tile", None),
        P("tm", "tile", None),
        P("tm", "tile", None),
        P("tm", "tile", None),
        P(None, "tile"),
        P(),
    )
    return jax.shard_map(
        body,
        mesh=mesh,
        in_specs=placed,
        out_specs=(P("tm", "tile", None), P("tm", "tile", None), P("tm", None, "tile")),
        check_vma=False,
    )
```
